512 devices in a mesh: dp: 4 (over y), seq: 16 (over z), section: 8 (over x, core).
Axes of the slice: x: 4, y: 4, z: 16, core: 2. Of those that a mesh axis runs over, the one named last changes fastest.
Arguments:
- signal: bfloat16 [4, 10240, 1280], P('dp', 'seq'), may hold values from -6 to 6
- kernel: bfloat16 [1536, 5, 1280], P('section'), may hold values from -0.078125 to 0.078125
- trunk_grad: bfloat16 [4, 5120, 1536], P('dp', ('seq', 'section')), may hold values from -24 to 24
Outputs:
- weight_grad: float32 [1536, 5, 1280], P(('section', 'seq'))
- input_grad: bfloat16 [4, 1280, 10240], P('dp', 'section', 'seq')
The draws below stay inside these ranges and needn't reach their ends.
All inputs are finite; a program needn't handle non-finite values.
Results may differ from the reference program's by a relative error of at most 0.019.
Values may be sent and summed in bfloat16 or wider, within the bound.
No kernel may reach another device: no remote copies, remote signals or barrier semaphores. Data moves between devices by JAX's collectives and lax.ppermute only.
A program may use at most 64 MiB of HBM per device.

```python
import jax
import jax.numpy as jnp
from jax import lax

C_IN = 1280
C_OUT = 1536
K = 5
L_DEV = 640
L = 10240
LOUT = 5120
CO_DEV = 192
N_DP = 4
N_SEQ = 16
N_SECTION = 8


def strengthened(entries, rng, source, target, shards_of, factor):
    owner, partner = [(jnp.arange(entries.shape[position]) // (entries.shape[position] // shards_of)).reshape([-1 if axis == position else 1 for axis in range(entries.ndim)]) for position in (source, target)]
    chosen = jax.random.permutation(rng, shards_of)[partner]
    strong = (owner == chosen) | (owner == (partner + shards_of // 2) % shards_of)
    return jnp.where(strong, factor * entries, entries)


def block_scale(own_key, extent, shards, least, high):
    loudness = 1.0
    for axis_at, blocks in shards:
        heights = jax.random.uniform(jax.random.fold_in(jax.random.fold_in(own_key, 6), axis_at), (blocks,), jnp.float32, least / len(shards), high / len(shards))
        loudness = loudness * jnp.repeat(jnp.exp(heights), extent[axis_at] // blocks).reshape((-1,) + (1,) * (len(extent) - 1 - axis_at))
    return loudness


def scatter_about(key, shape, spread, bound, split=(), held_as=jnp.bfloat16):
    drawn = jax.random.normal(key, shape, jnp.float32) * spread
    if len(split) > 0:
        drawn = block_scale(key, shape, split, -0.22, 0.18) * drawn
    return jnp.clip(drawn, min=-bound, max=bound).astype(held_as)


def gaussian_with(stream_key, shape, scale, reach, cuts, heavy, dtype=jnp.bfloat16):
    array = scale * jax.random.normal(stream_key, shape, jnp.float32)
    if cuts:
        array = array * block_scale(stream_key, shape, cuts, -0.22, 0.18)
    return jnp.clip(strengthened(array, jax.random.fold_in(stream_key, 3), *heavy), -reach, reach).astype(dtype)


def setup_inputs(seed: int = 0) -> dict:
    key_list = jax.random.split(jax.random.key(seed), 4)
    signal = scatter_about(key_list[0], (N_DP, L, C_IN), 1.0, 6.0, ((0, 4), (1, 16)))
    kernel = scatter_about(key_list[1], (C_OUT, K, C_IN), (K * C_IN) ** -0.5, 0.078125, ((0, 8),))
    trunk_grad = gaussian_with(key_list[2], (N_DP, LOUT, C_OUT), 1.0, 24.0, ((0, 4), (1, 128)), (1, 2, 128, 5.5))
    return dict(signal=signal, kernel=kernel, trunk_grad=trunk_grad)


def gelu_slope(values):
    normal_cdf = 0.5 * (1.0 + jax.scipy.special.erf(values * 0.7071067811865476))
    density = jnp.exp(-0.5 * values * values) * 0.3989422804014327
    return normal_cdf + values * density


def rounded(values):
    return lax.optimization_barrier(values.astype(jnp.bfloat16)).astype(jnp.float32)


def reference(signal, kernel, trunk_grad):
    weight_sum = jnp.zeros((C_OUT, K, C_IN), jnp.float32)
    input_grads = []
    for replica in range(N_DP):
        padded = jnp.pad(signal[replica], ((2, 2), (0, 0)))
        linear = jnp.zeros((L, C_OUT), jnp.float32)
        for offset in range(K):
            linear = linear + jnp.dot(padded[offset:offset + L], kernel[:, offset, :].T, preferred_element_type=jnp.float32)
        grad_hidden = 0.5 * jnp.repeat(trunk_grad[replica].astype(jnp.float32), 2, axis=0)
        grad_pre = (grad_hidden * gelu_slope(linear)).astype(jnp.bfloat16)
        for block in range(N_SEQ):
            begin = block * L_DEV
            grad_block = grad_pre[begin:begin + L_DEV]
            taps = []
            for offset in range(K):
                window = padded[begin + offset:begin + offset + L_DEV]
                taps.append(jnp.dot(grad_block.T, window, preferred_element_type=jnp.float32))
            weight_sum = weight_sum + rounded(jnp.stack(taps, axis=1))
        grad_padded = jnp.pad(grad_pre, ((2, 2), (0, 0)))
        input_sum = jnp.zeros((L, C_IN), jnp.float32)
        for group in range(N_SECTION):
            first_col = group * CO_DEV
            term = jnp.zeros((L, C_IN), jnp.float32)
            for offset in range(K):
                grad_slice = grad_padded[4 - offset:4 - offset + L, first_col:first_col + CO_DEV]
                kernel_slice = kernel[first_col:first_col + CO_DEV, offset, :]
                term = term + jnp.dot(grad_slice, kernel_slice, preferred_element_type=jnp.float32)
            input_sum = input_sum + rounded(term)
        input_grads.append(input_sum.T.astype(jnp.bfloat16))
    return weight_sum, jnp.stack(input_grads)
```

```python
import jax
import jax.numpy as jnp
from jax import lax
from jax.sharding import PartitionSpec as P


def extended(block, sides, width):
    for axis, dim in sides:
        count = lax.axis_size(axis)
        forward = [(i, i + 1) for i in range(count - 1)]
        backward = [(target, source) for source, target in forward]
        low = lax.ppermute(
            lax.slice_in_dim(block, block.shape[dim] - width, None, axis=dim), axis, forward
        )
        high = lax.ppermute(lax.slice_in_dim(block, 0, width, axis=dim), axis, backward)
        block = jnp.concatenate([low, block, high], axis=dim)
    return block


def gelu_slope(values):
    normal_cdf = 0.5 * (1.0 + jax.scipy.special.erf(values * 0.7071067811865476))
    density = jnp.exp(-0.5 * values * values) * 0.3989422804014327
    return normal_cdf + values * density


def convolve(padded, kernel, out_rows):
    linear = jnp.einsum(
        "lc,oc->lo", padded[0:out_rows], kernel[:, 0, :], preferred_element_type=jnp.float32
    )
    for offset in range(1, kernel.shape[1]):
        linear = linear + jnp.einsum(
            "lc,oc->lo",
            padded[offset : offset + out_rows],
            kernel[:, offset, :],
            preferred_element_type=jnp.float32,
        )
    return linear


def shards(signal, kernel, trunk_grad):
    local_signal = signal[0]
    length = local_signal.shape[0]
    taps_count = kernel.shape[1]
    out_ch = kernel.shape[0]
    in_ch = kernel.shape[2]
    n_section = lax.axis_size("section")
    rows = trunk_grad.shape[1]
    grouped = trunk_grad[0].reshape(rows, n_section, out_ch).transpose(1, 0, 2)
    pooled = lax.all_to_all(grouped, "section", 0, 0, tiled=True).reshape(rows * n_section, out_ch)
    padded = extended(local_signal, (("seq", 0),), 2)
    linear = convolve(padded, kernel, length)
    grad_hidden = 0.5 * jnp.repeat(pooled.astype(jnp.float32), 2, axis=0)
    grad_pre = (grad_hidden * gelu_slope(linear)).astype(jnp.bfloat16)
    grad_ext = extended(grad_pre, (("seq", 0),), 2)
    grad_middle = grad_ext[2 : 2 + length]
    taps = []
    for offset in range(taps_count):
        taps.append(
            jnp.einsum(
                "lo,lc->oc",
                grad_middle,
                padded[offset : offset + length],
                preferred_element_type=jnp.float32,
            ).astype(jnp.bfloat16)
        )
    n_seq = lax.axis_size("seq")
    partial = jnp.stack(taps, axis=1).reshape(n_seq, -1, 128)
    weight_part = lax.psum_scatter(partial, "seq", scatter_dimension=0, tiled=True)
    weight_rows = lax.psum(weight_part, "dp")
    weight_grad = weight_rows.reshape(-1, taps_count, in_ch).astype(jnp.float32)
    summed = jnp.einsum(
        "lo,oc->cl", grad_ext[4 : 4 + length], kernel[:, 0, :], preferred_element_type=jnp.float32
    )
    for offset in range(1, taps_count):
        summed = summed + jnp.einsum(
            "lo,oc->cl",
            grad_ext[4 - offset : 4 - offset + length],
            kernel[:, offset, :],
            preferred_element_type=jnp.float32,
        )
    input_rows = lax.psum_scatter(
        summed.astype(jnp.bfloat16), "section", scatter_dimension=0, tiled=True
    )
    return (weight_grad, input_rows[None])


def solution(mesh):
    return jax.shard_map(
        shards,
        mesh=mesh,
        in_specs=(
            P("dp", "seq", None),
            P("section", None, None),
            P("dp", ("seq", "section"), None),
        ),
        out_specs=(P(("section", "seq"), None, None), P("dp", "section", "seq")),
        check_vma=False,
    )
```

```python
import jax
import jax.numpy as jnp
from jax import lax
from jax.sharding import PartitionSpec as P


def extended(block, sides, width):
    for axis, dim in sides:
        count = lax.axis_size(axis)
        forward = [(i, i + 1) for i in range(count - 1)]
        backward = [(target, source) for source, target in forward]
        low = lax.ppermute(
            lax.slice_in_dim(block, block.shape[dim] - width, None, axis=dim), axis, forward
        )
        high = lax.ppermute(lax.slice_in_dim(block, 0, width, axis=dim), axis, backward)
        block = jnp.concatenate([low, block, high], axis=dim)
    return block


def gelu_slope(values):
    normal_cdf = 0.5 * (1.0 + jax.scipy.special.erf(values * 0.7071067811865476))
    density = jnp.exp(-0.5 * values * values) * 0.3989422804014327
    return normal_cdf + values * density


def convolve(padded, kernel, out_rows):
    linear = jnp.einsum(
        "lc,oc->lo", padded[0:out_rows], kernel[:, 0, :], preferred_element_type=jnp.float32
    )
    for offset in range(1, kernel.shape[1]):
        linear = linear + jnp.einsum(
            "lc,oc->lo",
            padded[offset : offset + out_rows],
            kernel[:, offset, :],
            preferred_element_type=jnp.float32,
        )
    return linear


def butterfly_sum(block, axis):
    count = lax.axis_size(axis)
    if count & (count - 1):
        return lax.psum(block.astype(jnp.float32), axis)
    total = block.astype(jnp.float32)
    step = 1
    while step < count:
        other = lax.ppermute(block if step == 1 else total, axis, [(i, i ^ step) for i in range(count)])
        total = total + other.astype(jnp.float32)
        step *= 2
    return total


def shards(signal, kernel, trunk_grad):
    local_signal = signal[0]
    length = local_signal.shape[0]
    taps_count = kernel.shape[1]
    out_ch = kernel.shape[0]
    in_ch = kernel.shape[2]
    n_section = lax.axis_size("section")
    rows = trunk_grad.shape[1]
    grouped = trunk_grad[0].reshape(rows, n_section, out_ch).transpose(1, 0, 2)
    pooled = lax.all_to_all(grouped, "section", 0, 0, tiled=True).reshape(rows * n_section, out_ch)
    padded = extended(local_signal, (("seq", 0),), 2)
    linear = convolve(padded, kernel, length)
    grad_hidden = 0.5 * jnp.repeat(pooled.astype(jnp.float32), 2, axis=0)
    grad_pre = (grad_hidden * gelu_slope(linear)).astype(jnp.bfloat16)
    grad_ext = extended(grad_pre, (("seq", 0),), 2)
    grad_middle = grad_ext[2 : 2 + length]
    taps = []
    for offset in range(taps_count):
        taps.append(
            jnp.einsum(
                "lo,lc->oc",
                grad_middle,
                padded[offset : offset + length],
                preferred_element_type=jnp.float32,
            ).astype(jnp.bfloat16)
        )
    n_seq = lax.axis_size("seq")
    partial = jnp.stack(taps, axis=1).reshape(n_seq, -1, 128)
    weight_part = lax.psum_scatter(partial, "seq", scatter_dimension=0, tiled=True)
    weight_rows = butterfly_sum(weight_part, "dp")
    weight_grad = weight_rows.reshape(-1, taps_count, in_ch)
    summed = jnp.einsum(
        "lo,oc->cl", grad_ext[4 : 4 + length], kernel[:, 0, :], preferred_element_type=jnp.float32
    )
    for offset in range(1, taps_count):
        summed = summed + jnp.einsum(
            "lo,oc->cl",
            grad_ext[4 - offset : 4 - offset + length],
            kernel[:, offset, :],
            preferred_element_type=jnp.float32,
        )
    groups = summed.astype(jnp.bfloat16).reshape(n_section, -1, length)
    received = lax.all_to_all(groups, "section", 0, 0, tiled=True)
    input_rows = jnp.sum(received.astype(jnp.float32), axis=0).astype(jnp.bfloat16)
    return (weight_grad, input_rows[None])


def solution(mesh):
    return jax.shard_map(
        shards,
        mesh=mesh,
        in_specs=(
            P("dp", "seq", None),
            P("section", None, None),
            P("dp", ("seq", "section"), None),
        ),
        out_specs=(P(("section", "seq"), None, None), P("dp", "section", "seq")),
        check_vma=False,
    )
```

```python
import jax
import jax.numpy as jnp
from jax import lax
from jax.sharding import PartitionSpec as P


def extended(block, sides, width):
    for axis, dim in sides:
        count = lax.axis_size(axis)
        forward = [(i, i + 1) for i in range(count - 1)]
        backward = [(target, source) for source, target in forward]
        low = lax.ppermute(
            lax.slice_in_dim(block, block.shape[dim] - width, None, axis=dim), axis, forward
        )
        high = lax.ppermute(lax.slice_in_dim(block, 0, width, axis=dim), axis, backward)
        block = jnp.concatenate([low, block, high], axis=dim)
    return block


def gelu_slope(values):
    normal_cdf = 0.5 * (1.0 + jax.scipy.special.erf(values * 0.7071067811865476))
    density = jnp.exp(-0.5 * values * values) * 0.3989422804014327
    return normal_cdf + values * density


def convolve(padded, kernel, out_rows):
    linear = jnp.einsum(
        "lc,oc->lo", padded[0:out_rows], kernel[:, 0, :], preferred_element_type=jnp.float32
    )
    for offset in range(1, kernel.shape[1]):
        linear = linear + jnp.einsum(
            "lc,oc->lo",
            padded[offset : offset + out_rows],
            kernel[:, offset, :],
            preferred_element_type=jnp.float32,
        )
    return linear


def butterfly_sum(block, axis):
    count = lax.axis_size(axis)
    if count & (count - 1):
        return lax.psum(block.astype(jnp.float32), axis)
    total = block.astype(jnp.float32)
    step = 1
    while step < count:
        other = lax.ppermute(block if step == 1 else total, axis, [(i, i ^ step) for i in range(count)])
        total = total + other.astype(jnp.float32)
        step *= 2
    return total


def shards(signal, kernel, trunk_grad):
    local_signal = signal[0]
    length = local_signal.shape[0]
    taps_count = kernel.shape[1]
    out_ch = kernel.shape[0]
    in_ch = kernel.shape[2]
    n_section = lax.axis_size("section")
    rows = trunk_grad.shape[1]
    grouped = trunk_grad[0].reshape(rows, n_section, out_ch).transpose(1, 0, 2)
    pooled = lax.all_to_all(grouped, "section", 0, 0, tiled=True).reshape(rows * n_section, out_ch)
    padded = extended(local_signal, (("seq", 0),), 2)
    linear = convolve(padded, kernel, length)
    grad_hidden = 0.5 * jnp.repeat(pooled.astype(jnp.float32), 2, axis=0)
    grad_pre = (grad_hidden * gelu_slope(linear)).astype(jnp.bfloat16)
    grad_ext = extended(grad_pre, (("seq", 0),), 2)
    grad_middle = grad_ext[2 : 2 + length]
    taps = []
    for offset in range(taps_count):
        taps.append(
            jnp.einsum(
                "lo,lc->oc",
                grad_middle,
                padded[offset : offset + length],
                preferred_element_type=jnp.float32,
            ).astype(jnp.bfloat16)
        )
    n_seq = lax.axis_size("seq")
    partial = jnp.stack(taps, axis=1).reshape(n_seq, -1, 128)
    weight_part = lax.psum_scatter(partial, "seq", scatter_dimension=0, tiled=True)
    weight_rows = jnp.sum(lax.all_gather(weight_part, "dp", axis=0, tiled=False).astype(jnp.float32), axis=0)
    weight_grad = weight_rows.reshape(-1, taps_count, in_ch)
    summed = jnp.einsum(
        "lo,oc->cl", grad_ext[4 : 4 + length], kernel[:, 0, :], preferred_element_type=jnp.float32
    )
    for offset in range(1, taps_count):
        summed = summed + jnp.einsum(
            "lo,oc->cl",
            grad_ext[4 - offset : 4 - offset + length],
            kernel[:, offset, :],
            preferred_element_type=jnp.float32,
        )
    groups = summed.astype(jnp.bfloat16).reshape(n_section, -1, length)
    received = lax.all_to_all(groups, "section", 0, 0, tiled=True)
    input_rows = jnp.sum(received.astype(jnp.float32), axis=0).astype(jnp.bfloat16)
    return (weight_grad, input_rows[None])


def solution(mesh):
    return jax.shard_map(
        shards,
        mesh=mesh,
        in_specs=(
            P("dp", "seq", None),
            P("section", None, None),
            P("dp", ("seq", "section"), None),
        ),
        out_specs=(P(("section", "seq"), None, None), P("dp", "section", "seq")),
        check_vma=False,
    )
```

```python
import jax
import jax.numpy as jnp
from jax import lax
from jax.sharding import PartitionSpec as P


def extended(block, sides, width):
    for axis, dim in sides:
        count = lax.axis_size(axis)
        forward = [(i, i + 1) for i in range(count - 1)]
        backward = [(target, source) for source, target in forward]
        low = lax.ppermute(
            lax.slice_in_dim(block, block.shape[dim] - width, None, axis=dim), axis, forward
        )
        high = lax.ppermute(lax.slice_in_dim(block, 0, width, axis=dim), axis, backward)
        block = jnp.concatenate([low, block, high], axis=dim)
    return block


def gelu_slope(values):
    normal_cdf = 0.5 * (1.0 + jax.scipy.special.erf(values * 0.7071067811865476))
    density = jnp.exp(-0.5 * values * values) * 0.3989422804014327
    return normal_cdf + values * density


def convolve(padded, kernel, out_rows):
    linear = jnp.einsum(
        "lc,oc->lo", padded[0:out_rows], kernel[:, 0, :], preferred_element_type=jnp.float32
    )
    for offset in range(1, kernel.shape[1]):
        linear = linear + jnp.einsum(
            "lc,oc->lo",
            padded[offset : offset + out_rows],
            kernel[:, offset, :],
            preferred_element_type=jnp.float32,
        )
    return linear


def butterfly_sum(block, axis):
    count = lax.axis_size(axis)
    if count & (count - 1):
        return lax.psum(block.astype(jnp.float32), axis)
    total = block.astype(jnp.float32)
    step = 1
    while step < count:
        other = lax.ppermute(block if step == 1 else total, axis, [(i, i ^ step) for i in range(count)])
        total = total + other.astype(jnp.float32)
        step *= 2
    return total


def symmetric_sum(block, axis):
    count = lax.axis_size(axis)
    if count & (count - 1):
        return lax.psum(block.astype(jnp.float32), axis)
    parts = [block] + [
        lax.ppermute(block, axis, [(i, i ^ step) for i in range(count)]) for step in range(1, count)
    ]
    parts = [part.astype(jnp.float32) for part in parts]
    while len(parts) > 1:
        parts = [parts[i] + parts[i + 1] for i in range(0, len(parts), 2)]
    return parts[0]


def shards(signal, kernel, trunk_grad):
    local_signal = signal[0]
    length = local_signal.shape[0]
    taps_count = kernel.shape[1]
    out_ch = kernel.shape[0]
    in_ch = kernel.shape[2]
    n_section = lax.axis_size("section")
    rows = trunk_grad.shape[1]
    grouped = trunk_grad[0].reshape(rows, n_section, out_ch).transpose(1, 0, 2)
    pooled = lax.all_to_all(grouped, "section", 0, 0, tiled=True).reshape(rows * n_section, out_ch)
    padded = extended(local_signal, (("seq", 0),), 2)
    linear = convolve(padded, kernel, length)
    grad_hidden = 0.5 * jnp.repeat(pooled.astype(jnp.float32), 2, axis=0)
    grad_pre = (grad_hidden * gelu_slope(linear)).astype(jnp.bfloat16)
    grad_ext = extended(grad_pre, (("seq", 0),), 2)
    grad_middle = grad_ext[2 : 2 + length]
    n_seq = lax.axis_size("seq")
    chunk = out_ch // n_seq * taps_count
    chunk_rows = -(-chunk // 16) * 16
    shifted = jnp.stack(
        [jnp.pad(grad_middle.T, ((0, 0), (k, taps_count - 1 - k))) for k in range(taps_count)],
        axis=1,
    ).reshape(n_seq, chunk, length + taps_count - 1)
    banded = jnp.pad(shifted, ((0, 0), (0, chunk_rows - chunk), (0, 0))).reshape(
        n_seq * chunk_rows, length + taps_count - 1
    )
    partial = jnp.dot(banded, padded, preferred_element_type=jnp.float32).astype(jnp.bfloat16)
    weight_part = lax.psum_scatter(
        partial.reshape(n_seq, chunk_rows, in_ch), "seq", scatter_dimension=0, tiled=True
    )[0, :chunk]
    weight_grad = symmetric_sum(weight_part, "dp").reshape(-1, taps_count, in_ch)
    summed = jnp.einsum(
        "lo,oc->cl", grad_ext[4 : 4 + length], kernel[:, 0, :], preferred_element_type=jnp.float32
    )
    for offset in range(1, taps_count):
        summed = summed + jnp.einsum(
            "lo,oc->cl",
            grad_ext[4 - offset : 4 - offset + length],
            kernel[:, offset, :],
            preferred_element_type=jnp.float32,
        )
    groups = summed.astype(jnp.bfloat16).reshape(n_section, -1, length)
    received = lax.all_to_all(groups, "section", 0, 0, tiled=True)
    input_rows = jnp.sum(received.astype(jnp.float32), axis=0).astype(jnp.bfloat16)
    return (weight_grad, input_rows[None])


def solution(mesh):
    return jax.shard_map(
        shards,
        mesh=mesh,
        in_specs=(
            P("dp", "seq", None),
            P("section", None, None),
            P("dp", ("seq", "section"), None),
        ),
        out_specs=(P(("section", "seq"), None, None), P("dp", "section", "seq")),
        check_vma=False,
    )
```

```python
import jax
import jax.numpy as jnp
from jax import lax
from jax.sharding import PartitionSpec as P


def extended(block, sides, width):
    for axis, dim in sides:
        count = lax.axis_size(axis)
        forward = [(i, i + 1) for i in range(count - 1)]
        backward = [(target, source) for source, target in forward]
        low = lax.ppermute(
            lax.slice_in_dim(block, block.shape[dim] - width, None, axis=dim), axis, forward
        )
        high = lax.ppermute(lax.slice_in_dim(block, 0, width, axis=dim), axis, backward)
        block = jnp.concatenate([low, block, high], axis=dim)
    return block


def gelu_slope(values):
    normal_cdf = 0.5 * (1.0 + jax.scipy.special.erf(values * 0.7071067811865476))
    density = jnp.exp(-0.5 * values * values) * 0.3989422804014327
    return normal_cdf + values * density


def convolve(padded, kernel, out_rows):
    linear = jnp.einsum(
        "lc,oc->lo", padded[0:out_rows], kernel[:, 0, :], preferred_element_type=jnp.float32
    )
    for offset in range(1, kernel.shape[1]):
        linear = linear + jnp.einsum(
            "lc,oc->lo",
            padded[offset : offset + out_rows],
            kernel[:, offset, :],
            preferred_element_type=jnp.float32,
        )
    return linear


def butterfly_sum(block, axis):
    count = lax.axis_size(axis)
    if count & (count - 1):
        return lax.psum(block.astype(jnp.float32), axis)
    total = block.astype(jnp.float32)
    step = 1
    while step < count:
        other = lax.ppermute(block if step == 1 else total, axis, [(i, i ^ step) for i in range(count)])
        total = total + other.astype(jnp.float32)
        step *= 2
    return total


def symmetric_sum(block, axis):
    count = lax.axis_size(axis)
    if count & (count - 1):
        return lax.psum(block.astype(jnp.float32), axis)
    parts = [block] + [
        lax.ppermute(block, axis, [(i, i ^ step) for i in range(count)]) for step in range(1, count)
    ]
    parts = [part.astype(jnp.float32) for part in parts]
    while len(parts) > 1:
        parts = [parts[i] + parts[i + 1] for i in range(0, len(parts), 2)]
    return parts[0]


def shards(signal, kernel, trunk_grad):
    local_signal = signal[0]
    length = local_signal.shape[0]
    taps_count = kernel.shape[1]
    out_ch = kernel.shape[0]
    in_ch = kernel.shape[2]
    n_section = lax.axis_size("section")
    rows = trunk_grad.shape[1]
    grouped = trunk_grad[0].reshape(rows, n_section, out_ch).transpose(1, 0, 2)
    pooled = lax.all_to_all(grouped, "section", 0, 0, tiled=True).reshape(rows * n_section, out_ch)
    padded = extended(local_signal, (("seq", 0),), 2)
    stacked = kernel.transpose(1, 0, 2).reshape(taps_count * out_ch, in_ch)
    per_tap = jnp.einsum("tc,jc->tj", padded, stacked, preferred_element_type=jnp.float32)
    linear = per_tap[0:length, 0:out_ch]
    for k in range(1, taps_count):
        linear = linear + per_tap[k : k + length, k * out_ch : (k + 1) * out_ch]
    grad_hidden = 0.5 * jnp.repeat(pooled.astype(jnp.float32), 2, axis=0)
    grad_pre = (grad_hidden * gelu_slope(linear)).astype(jnp.bfloat16)
    grad_ext = extended(grad_pre, (("seq", 0),), 2)
    grad_middle = grad_ext[2 : 2 + length]
    n_seq = lax.axis_size("seq")
    chunk = out_ch // n_seq * taps_count
    chunk_rows = -(-chunk // 16) * 16
    shifted = jnp.stack(
        [jnp.pad(grad_middle.T, ((0, 0), (k, taps_count - 1 - k))) for k in range(taps_count)],
        axis=1,
    ).reshape(n_seq, chunk, length + taps_count - 1)
    banded = jnp.pad(shifted, ((0, 0), (0, chunk_rows - chunk), (0, 0))).reshape(
        n_seq * chunk_rows, length + taps_count - 1
    )
    partial = jnp.dot(banded, padded, preferred_element_type=jnp.float32).astype(jnp.bfloat16)
    weight_part = lax.psum_scatter(
        partial.reshape(n_seq, chunk_rows, in_ch), "seq", scatter_dimension=0, tiled=True
    )[0, :chunk]
    n_dp = lax.axis_size("dp")
    copies = lax.all_to_all(
        jnp.broadcast_to(weight_part[None], (n_dp,) + weight_part.shape), "dp", 0, 0, tiled=True
    ).astype(jnp.float32)
    total = copies[0]
    for j in range(1, n_dp):
        total = total + copies[j]
    weight_grad = total.reshape(-1, taps_count, in_ch)
    summed = jnp.einsum(
        "lo,oc->cl", grad_ext[4 : 4 + length], kernel[:, 0, :], preferred_element_type=jnp.float32
    )
    for offset in range(1, taps_count):
        summed = summed + jnp.einsum(
            "lo,oc->cl",
            grad_ext[4 - offset : 4 - offset + length],
            kernel[:, offset, :],
            preferred_element_type=jnp.float32,
        )
    groups = summed.astype(jnp.bfloat16).reshape(n_section, -1, length)
    received = lax.all_to_all(groups, "section", 0, 0, tiled=True)
    input_rows = jnp.sum(received.astype(jnp.float32), axis=0).astype(jnp.bfloat16)
    return (weight_grad, input_rows[None])


def solution(mesh):
    return jax.shard_map(
        shards,
        mesh=mesh,
        in_specs=(
            P("dp", "seq", None),
            P("section", None, None),
            P("dp", ("seq", "section"), None),
        ),
        out_specs=(P(("section", "seq"), None, None), P("dp", "section", "seq")),
        check_vma=False,
    )
```

```python
import jax
import jax.numpy as jnp
from jax import lax
from jax.sharding import PartitionSpec as P


def extended(block, sides, width):
    for axis, dim in sides:
        count = lax.axis_size(axis)
        forward = [(i, i + 1) for i in range(count - 1)]
        backward = [(target, source) for source, target in forward]
        low = lax.ppermute(
            lax.slice_in_dim(block, block.shape[dim] - width, None, axis=dim), axis, forward
        )
        high = lax.ppermute(lax.slice_in_dim(block, 0, width, axis=dim), axis, backward)
        block = jnp.concatenate([low, block, high], axis=dim)
    return block


def gelu_slope(values):
    normal_cdf = 0.5 * (1.0 + jax.scipy.special.erf(values * 0.7071067811865476))
    density = jnp.exp(-0.5 * values * values) * 0.3989422804014327
    return normal_cdf + values * density


def convolve(padded, kernel, out_rows):
    linear = jnp.einsum(
        "lc,oc->lo", padded[0:out_rows], kernel[:, 0, :], preferred_element_type=jnp.float32
    )
    for offset in range(1, kernel.shape[1]):
        linear = linear + jnp.einsum(
            "lc,oc->lo",
            padded[offset : offset + out_rows],
            kernel[:, offset, :],
            preferred_element_type=jnp.float32,
        )
    return linear


def butterfly_sum(block, axis):
    count = lax.axis_size(axis)
    if count & (count - 1):
        return lax.psum(block.astype(jnp.float32), axis)
    total = block.astype(jnp.float32)
    step = 1
    while step < count:
        other = lax.ppermute(block if step == 1 else total, axis, [(i, i ^ step) for i in range(count)])
        total = total + other.astype(jnp.float32)
        step *= 2
    return total


def symmetric_sum(block, axis):
    count = lax.axis_size(axis)
    if count & (count - 1):
        return lax.psum(block.astype(jnp.float32), axis)
    parts = [block] + [
        lax.ppermute(block, axis, [(i, i ^ step) for i in range(count)]) for step in range(1, count)
    ]
    parts = [part.astype(jnp.float32) for part in parts]
    while len(parts) > 1:
        parts = [parts[i] + parts[i + 1] for i in range(0, len(parts), 2)]
    return parts[0]


def shards(signal, kernel, trunk_grad):
    local_signal = signal[0]
    length = local_signal.shape[0]
    taps_count = kernel.shape[1]
    out_ch = kernel.shape[0]
    in_ch = kernel.shape[2]
    n_section = lax.axis_size("section")
    rows = trunk_grad.shape[1]
    grouped = jnp.repeat(trunk_grad[0].reshape(rows, n_section, out_ch), 2, axis=0).transpose(1, 0, 2)
    upsampled = lax.all_to_all(grouped, "section", 0, 0, tiled=True).reshape(2 * rows * n_section, out_ch)
    padded = extended(local_signal, (("seq", 0),), 2)
    stacked = kernel.transpose(1, 0, 2).reshape(taps_count * out_ch, in_ch)
    per_tap = jnp.einsum("tc,jc->tj", padded, stacked, preferred_element_type=jnp.float32)
    linear = per_tap[0:length, 0:out_ch]
    for k in range(1, taps_count):
        linear = linear + per_tap[k : k + length, k * out_ch : (k + 1) * out_ch]
    grad_hidden = 0.5 * upsampled.astype(jnp.float32)
    grad_pre = (grad_hidden * gelu_slope(linear)).astype(jnp.bfloat16)
    grad_ext = extended(grad_pre, (("seq", 0),), 2)
    grad_middle = grad_ext[2 : 2 + length]
    n_seq = lax.axis_size("seq")
    own = out_ch // n_seq
    own_rows = -(-own // 16) * 16
    spread = jnp.pad(grad_middle.T.reshape(n_seq, own, length), ((0, 0), (0, own_rows - own), (0, 0)))
    banded = jnp.concatenate(
        [jnp.pad(spread, ((0, 0), (0, 0), (k, taps_count - 1 - k))) for k in range(taps_count)],
        axis=1,
    ).reshape(n_seq * taps_count * own_rows, length + taps_count - 1)
    partial = jnp.dot(banded, padded, preferred_element_type=jnp.float32).astype(jnp.bfloat16)
    partial = partial.reshape(n_seq, taps_count * own_rows, in_ch)
    weight_part = lax.psum_scatter(partial, "seq", scatter_dimension=0, tiled=True)[0]
    n_dp = lax.axis_size("dp")
    copies = lax.all_to_all(
        jnp.broadcast_to(weight_part[None], (n_dp,) + weight_part.shape), "dp", 0, 0, tiled=True
    ).astype(jnp.float32)
    total = copies[0]
    for j in range(1, n_dp):
        total = total + copies[j]
    weight_grad = total.reshape(taps_count, own_rows, in_ch)[:, :own].transpose(1, 0, 2)
    summed = jnp.einsum(
        "lo,oc->cl", grad_ext[4 : 4 + length], kernel[:, 0, :], preferred_element_type=jnp.float32
    )
    for offset in range(1, taps_count):
        summed = summed + jnp.einsum(
            "lo,oc->cl",
            grad_ext[4 - offset : 4 - offset + length],
            kernel[:, offset, :],
            preferred_element_type=jnp.float32,
        )
    groups = summed.astype(jnp.bfloat16).reshape(n_section, -1, length)
    received = lax.all_to_all(groups, "section", 0, 0, tiled=True)
    input_rows = jnp.sum(received.astype(jnp.float32), axis=0).astype(jnp.bfloat16)
    return (weight_grad, input_rows[None])


def solution(mesh):
    return jax.shard_map(
        shards,
        mesh=mesh,
        in_specs=(
            P("dp", "seq", None),
            P("section", None, None),
            P("dp", ("seq", "section"), None),
        ),
        out_specs=(P(("section", "seq"), None, None), P("dp", "section", "seq")),
        check_vma=False,
    )
```

```python
import jax
import jax.numpy as jnp
from jax import lax
from jax.sharding import PartitionSpec as P


def extended(block, sides, width):
    for axis, dim in sides:
        count = lax.axis_size(axis)
        forward = [(i, i + 1) for i in range(count - 1)]
        backward = [(target, source) for source, target in forward]
        low = lax.ppermute(
            lax.slice_in_dim(block, block.shape[dim] - width, None, axis=dim), axis, forward
        )
        high = lax.ppermute(lax.slice_in_dim(block, 0, width, axis=dim), axis, backward)
        block = jnp.concatenate([low, block, high], axis=dim)
    return block


def gelu_slope(values):
    normal_cdf = 0.5 * (1.0 + jax.scipy.special.erf(values * 0.7071067811865476))
    density = jnp.exp(-0.5 * values * values) * 0.3989422804014327
    return normal_cdf + values * density


def convolve(padded, kernel, out_rows):
    linear = jnp.einsum(
        "lc,oc->lo", padded[0:out_rows], kernel[:, 0, :], preferred_element_type=jnp.float32
    )
    for offset in range(1, kernel.shape[1]):
        linear = linear + jnp.einsum(
            "lc,oc->lo",
            padded[offset : offset + out_rows],
            kernel[:, offset, :],
            preferred_element_type=jnp.float32,
        )
    return linear


def butterfly_sum(block, axis):
    count = lax.axis_size(axis)
    if count & (count - 1):
        return lax.psum(block.astype(jnp.float32), axis)
    total = block.astype(jnp.float32)
    step = 1
    while step < count:
        other = lax.ppermute(block if step == 1 else total, axis, [(i, i ^ step) for i in range(count)])
        total = total + other.astype(jnp.float32)
        step *= 2
    return total


def symmetric_sum(block, axis):
    count = lax.axis_size(axis)
    if count & (count - 1):
        return lax.psum(block.astype(jnp.float32), axis)
    parts = [block] + [
        lax.ppermute(block, axis, [(i, i ^ step) for i in range(count)]) for step in range(1, count)
    ]
    parts = [part.astype(jnp.float32) for part in parts]
    while len(parts) > 1:
        parts = [parts[i] + parts[i + 1] for i in range(0, len(parts), 2)]
    return parts[0]


def shards(signal, kernel, trunk_grad):
    local_signal = signal[0]
    length = local_signal.shape[0]
    taps_count = kernel.shape[1]
    out_ch = kernel.shape[0]
    in_ch = kernel.shape[2]
    n_section = lax.axis_size("section")
    rows = trunk_grad.shape[1]
    grouped = jnp.repeat(trunk_grad[0].reshape(rows, n_section, out_ch), 2, axis=0).transpose(1, 0, 2)
    upsampled = lax.all_to_all(grouped, "section", 0, 0, tiled=True).reshape(2 * rows * n_section, out_ch)
    padded = extended(local_signal, (("seq", 0),), 2)
    stacked = kernel.transpose(1, 0, 2).reshape(taps_count * out_ch, in_ch)
    per_tap = jnp.einsum("tc,jc->tj", padded, stacked, preferred_element_type=jnp.float32)
    linear = per_tap[0:length, 0:out_ch]
    for k in range(1, taps_count):
        linear = linear + per_tap[k : k + length, k * out_ch : (k + 1) * out_ch]
    grad_hidden = 0.5 * upsampled.astype(jnp.float32)
    grad_pre = (grad_hidden * gelu_slope(linear)).astype(jnp.bfloat16)
    grad_ext = extended(grad_pre, (("seq", 0),), 2)
    grad_middle = grad_ext[2 : 2 + length]
    n_seq = lax.axis_size("seq")
    own = out_ch // n_seq
    own_rows = -(-own // 16) * 16
    spread = jnp.pad(grad_middle.T.reshape(n_seq, own, length), ((0, 0), (0, own_rows - own), (0, 0)))
    banded = jnp.concatenate(
        [jnp.pad(spread, ((0, 0), (0, 0), (k, taps_count - 1 - k))) for k in range(taps_count)],
        axis=1,
    ).reshape(n_seq * taps_count * own_rows, length + taps_count - 1)
    partial = jnp.dot(banded, padded, preferred_element_type=jnp.float32).astype(jnp.bfloat16)
    partial = partial.reshape(n_seq, taps_count * own_rows, in_ch)
    weight_part = lax.psum_scatter(partial, "seq", scatter_dimension=0, tiled=True)[0]
    n_dp = lax.axis_size("dp")
    copies = lax.all_gather(weight_part, "dp", axis=0, tiled=False).astype(jnp.float32)
    total = copies[0]
    for j in range(1, n_dp):
        total = total + copies[j]
    weight_grad = total.reshape(taps_count, own_rows, in_ch)[:, :own].transpose(1, 0, 2)
    summed = jnp.einsum(
        "lo,oc->cl", grad_ext[4 : 4 + length], kernel[:, 0, :], preferred_element_type=jnp.float32
    )
    for offset in range(1, taps_count):
        summed = summed + jnp.einsum(
            "lo,oc->cl",
            grad_ext[4 - offset : 4 - offset + length],
            kernel[:, offset, :],
            preferred_element_type=jnp.float32,
        )
    groups = summed.astype(jnp.bfloat16).reshape(n_section, -1, length)
    received = lax.all_to_all(groups, "section", 0, 0, tiled=True)
    input_rows = jnp.sum(received.astype(jnp.float32), axis=0).astype(jnp.bfloat16)
    return (weight_grad, input_rows[None])


def solution(mesh):
    return jax.shard_map(
        shards,
        mesh=mesh,
        in_specs=(
            P("dp", "seq", None),
            P("section", None, None),
            P("dp", ("seq", "section"), None),
        ),
        out_specs=(P(("section", "seq"), None, None), P("dp", "section", "seq")),
        check_vma=False,
    )
```

```python
import jax
import jax.numpy as jnp
from jax import lax
from jax.sharding import PartitionSpec as P


def extended(block, sides, width):
    for axis, dim in sides:
        count = lax.axis_size(axis)
        forward = [(i, i + 1) for i in range(count - 1)]
        backward = [(target, source) for source, target in forward]
        low = lax.ppermute(
            lax.slice_in_dim(block, block.shape[dim] - width, None, axis=dim), axis, forward
        )
        high = lax.ppermute(lax.slice_in_dim(block, 0, width, axis=dim), axis, backward)
        block = jnp.concatenate([low, block, high], axis=dim)
    return block


def gelu_slope(values):
    normal_cdf = 0.5 * (1.0 + jax.scipy.special.erf(values * 0.7071067811865476))
    density = jnp.exp(-0.5 * values * values) * 0.3989422804014327
    return normal_cdf + values * density


def convolve(padded, kernel, out_rows):
    linear = jnp.einsum(
        "lc,oc->lo", padded[0:out_rows], kernel[:, 0, :], preferred_element_type=jnp.float32
    )
    for offset in range(1, kernel.shape[1]):
        linear = linear + jnp.einsum(
            "lc,oc->lo",
            padded[offset : offset + out_rows],
            kernel[:, offset, :],
            preferred_element_type=jnp.float32,
        )
    return linear


def butterfly_sum(block, axis):
    count = lax.axis_size(axis)
    if count & (count - 1):
        return lax.psum(block.astype(jnp.float32), axis)
    total = block.astype(jnp.float32)
    step = 1
    while step < count:
        other = lax.ppermute(block if step == 1 else total, axis, [(i, i ^ step) for i in range(count)])
        total = total + other.astype(jnp.float32)
        step *= 2
    return total


def symmetric_sum(block, axis):
    count = lax.axis_size(axis)
    if count & (count - 1):
        return lax.psum(block.astype(jnp.float32), axis)
    parts = [block] + [
        lax.ppermute(block, axis, [(i, i ^ step) for i in range(count)]) for step in range(1, count)
    ]
    parts = [part.astype(jnp.float32) for part in parts]
    while len(parts) > 1:
        parts = [parts[i] + parts[i + 1] for i in range(0, len(parts), 2)]
    return parts[0]


def shards(signal, kernel, trunk_grad):
    local_signal = signal[0]
    length = local_signal.shape[0]
    taps_count = kernel.shape[1]
    out_ch = kernel.shape[0]
    in_ch = kernel.shape[2]
    n_section = lax.axis_size("section")
    rows = trunk_grad.shape[1]
    grouped = jnp.repeat(trunk_grad[0].reshape(rows, n_section, out_ch), 2, axis=0).transpose(1, 0, 2)
    upsampled = lax.all_to_all(grouped, "section", 0, 0, tiled=True).reshape(2 * rows * n_section, out_ch)
    padded = extended(local_signal, (("seq", 0),), 2)
    stacked = kernel.transpose(1, 0, 2).reshape(taps_count * out_ch, in_ch)
    per_tap = jnp.einsum("tc,jc->tj", padded, stacked, preferred_element_type=jnp.float32)
    linear = per_tap[0:length, 0:out_ch]
    for k in range(1, taps_count):
        linear = linear + per_tap[k : k + length, k * out_ch : (k + 1) * out_ch]
    grad_hidden = 0.5 * upsampled.astype(jnp.float32)
    grad_pre = (grad_hidden * gelu_slope(linear)).astype(jnp.bfloat16)
    grad_ext = extended(grad_pre, (("seq", 0),), 2)
    grad_middle = grad_ext[2 : 2 + length]
    n_seq = lax.axis_size("seq")
    own = out_ch // n_seq
    chunk = own * taps_count
    chunk_rows = -(-chunk // 16) * 16
    spread = grad_middle.T.reshape(n_seq, own, length)
    blocks = [jnp.pad(spread, ((0, 0), (0, 0), (k, taps_count - 1 - k))) for k in range(taps_count)]
    blocks.append(jnp.zeros((n_seq, chunk_rows - chunk, length + taps_count - 1), spread.dtype))
    banded = jnp.concatenate(blocks, axis=1).reshape(n_seq * chunk_rows, length + taps_count - 1)
    partial = jnp.dot(banded, padded, preferred_element_type=jnp.float32).astype(jnp.bfloat16)
    partial = partial.reshape(n_seq, chunk_rows, in_ch)
    weight_part = lax.psum_scatter(partial, "seq", scatter_dimension=0, tiled=True)[0]
    n_dp = lax.axis_size("dp")
    copies = lax.all_gather(weight_part, "dp", axis=0, tiled=False).astype(jnp.float32)
    total = copies[0]
    for j in range(1, n_dp):
        total = total + copies[j]
    weight_grad = total[:chunk].reshape(taps_count, own, in_ch).transpose(1, 0, 2)
    summed = jnp.einsum(
        "lo,oc->cl", grad_ext[4 : 4 + length], kernel[:, 0, :], preferred_element_type=jnp.float32
    )
    for offset in range(1, taps_count):
        summed = summed + jnp.einsum(
            "lo,oc->cl",
            grad_ext[4 - offset : 4 - offset + length],
            kernel[:, offset, :],
            preferred_element_type=jnp.float32,
        )
    groups = summed.astype(jnp.bfloat16).reshape(n_section, -1, length)
    received = lax.all_to_all(groups, "section", 0, 0, tiled=True)
    input_rows = jnp.sum(received.astype(jnp.float32), axis=0).astype(jnp.bfloat16)
    return (weight_grad, input_rows[None])


def solution(mesh):
    return jax.shard_map(
        shards,
        mesh=mesh,
        in_specs=(
            P("dp", "seq", None),
            P("section", None, None),
            P("dp", ("seq", "section"), None),
        ),
        out_specs=(P(("section", "seq"), None, None), P("dp", "section", "seq")),
        check_vma=False,
    )
```

```python
import jax
import jax.numpy as jnp
from jax import lax
from jax.sharding import PartitionSpec as P


def extended(block, sides, width):
    for axis, dim in sides:
        count = lax.axis_size(axis)
        forward = [(i, i + 1) for i in range(count - 1)]
        backward = [(target, source) for source, target in forward]
        low = lax.ppermute(
            lax.slice_in_dim(block, block.shape[dim] - width, None, axis=dim), axis, forward
        )
        high = lax.ppermute(lax.slice_in_dim(block, 0, width, axis=dim), axis, backward)
        block = jnp.concatenate([low, block, high], axis=dim)
    return block


def gelu_slope(values):
    normal_cdf = 0.5 * (1.0 + jax.scipy.special.erf(values * 0.7071067811865476))
    density = jnp.exp(-0.5 * values * values) * 0.3989422804014327
    return normal_cdf + values * density


def shards(signal, kernel, trunk_grad):
    local_signal = signal[0]
    length = local_signal.shape[0]
    taps_count = kernel.shape[1]
    out_ch = kernel.shape[0]
    in_ch = kernel.shape[2]
    n_section = lax.axis_size("section")
    rows = trunk_grad.shape[1]
    grouped = jnp.repeat(trunk_grad[0].reshape(rows, n_section, out_ch), 2, axis=0).transpose(1, 0, 2)
    upsampled = lax.all_to_all(grouped, "section", 0, 0, tiled=True).reshape(2 * rows * n_section, out_ch)
    padded = extended(local_signal, (("seq", 0),), 2)
    stacked = kernel.transpose(1, 0, 2).reshape(taps_count * out_ch, in_ch)
    per_tap = jnp.einsum("tc,jc->tj", padded, stacked, preferred_element_type=jnp.float32)
    linear = per_tap[0:length, 0:out_ch]
    for k in range(1, taps_count):
        linear = linear + per_tap[k : k + length, k * out_ch : (k + 1) * out_ch]
    grad_hidden = 0.5 * upsampled.astype(jnp.float32)
    grad_pre = (grad_hidden * gelu_slope(linear)).astype(jnp.bfloat16)
    grad_ext = extended(grad_pre, (("seq", 0),), 2)
    grad_middle = grad_ext[2 : 2 + length]
    n_seq = lax.axis_size("seq")
    own = out_ch // n_seq
    own_rows = -(-own // 16) * 16
    spread = jnp.pad(grad_middle.T.reshape(n_seq, own, length), ((0, 0), (0, own_rows - own), (0, 0)))
    banded = jnp.concatenate(
        [jnp.pad(spread, ((0, 0), (0, 0), (k, taps_count - 1 - k))) for k in range(taps_count)],
        axis=1,
    ).reshape(n_seq * taps_count * own_rows, length + taps_count - 1)
    partial = jnp.dot(banded, padded, preferred_element_type=jnp.float32).astype(jnp.bfloat16)
    partial = partial.reshape(n_seq, taps_count * own_rows, in_ch)
    weight_part = lax.psum_scatter(partial, "seq", scatter_dimension=0, tiled=True)[0]
    n_dp = lax.axis_size("dp")
    copies = lax.all_gather(weight_part, "dp", axis=0, tiled=False).astype(jnp.float32)
    total = copies[0]
    for j in range(1, n_dp):
        total = total + copies[j]
    weight_grad = total.reshape(taps_count, own_rows, in_ch)[:, :own].transpose(1, 0, 2)
    summed = jnp.einsum(
        "lo,oc->cl", grad_ext[4 : 4 + length], kernel[:, 0, :], preferred_element_type=jnp.float32
    )
    for offset in range(1, taps_count):
        summed = summed + jnp.einsum(
            "lo,oc->cl",
            grad_ext[4 - offset : 4 - offset + length],
            kernel[:, offset, :],
            preferred_element_type=jnp.float32,
        )
    groups = summed.astype(jnp.bfloat16).reshape(n_section, -1, length)
    received = lax.all_to_all(groups, "section", 0, 0, tiled=True)
    input_rows = jnp.sum(received.astype(jnp.float32), axis=0).astype(jnp.bfloat16)
    return (weight_grad, input_rows[None])


def solution(mesh):
    return jax.shard_map(
        shards,
        mesh=mesh,
        in_specs=(
            P("dp", "seq", None),
            P("section", None, None),
            P("dp", ("seq", "section"), None),
        ),
        out_specs=(P(("section", "seq"), None, None), P("dp", "section", "seq")),
        check_vma=False,
    )
```

```python
import jax
import jax.numpy as jnp
from jax import lax
from jax.sharding import PartitionSpec as P


def extended(block, sides, width):
    for axis, dim in sides:
        count = lax.axis_size(axis)
        forward = [(i, i + 1) for i in range(count - 1)]
        backward = [(target, source) for source, target in forward]
        low = lax.ppermute(
            lax.slice_in_dim(block, block.shape[dim] - width, None, axis=dim), axis, forward
        )
        high = lax.ppermute(lax.slice_in_dim(block, 0, width, axis=dim), axis, backward)
        block = jnp.concatenate([low, block, high], axis=dim)
    return block


def gelu_slope(values):
    normal_cdf = 0.5 * (1.0 + jax.scipy.special.erf(values * 0.7071067811865476))
    density = jnp.exp(-0.5 * values * values) * 0.3989422804014327
    return normal_cdf + values * density


def shards(signal, kernel, trunk_grad):
    local_signal = signal[0]
    length = local_signal.shape[0]
    taps_count = kernel.shape[1]
    out_ch = kernel.shape[0]
    in_ch = kernel.shape[2]
    n_section = lax.axis_size("section")
    rows = trunk_grad.shape[1]
    grouped = jnp.repeat(trunk_grad[0].reshape(rows, n_section, out_ch), 2, axis=0).transpose(1, 0, 2)
    dense = grouped.reshape(n_section, -1, 128)
    upsampled = lax.all_to_all(dense, "section", 0, 0, tiled=True).reshape(2 * rows * n_section, out_ch)
    padded = extended(local_signal, (("seq", 0),), 2)
    stacked = kernel.transpose(1, 0, 2).reshape(taps_count * out_ch, in_ch)
    per_tap = jnp.einsum("tc,jc->tj", padded, stacked, preferred_element_type=jnp.float32)
    linear = per_tap[0:length, 0:out_ch]
    for k in range(1, taps_count):
        linear = linear + per_tap[k : k + length, k * out_ch : (k + 1) * out_ch]
    grad_hidden = 0.5 * upsampled.astype(jnp.float32)
    grad_pre = (grad_hidden * gelu_slope(linear)).astype(jnp.bfloat16)
    grad_ext = extended(grad_pre, (("seq", 0),), 2)
    grad_middle = grad_ext[2 : 2 + length]
    n_seq = lax.axis_size("seq")
    own = out_ch // n_seq
    own_rows = -(-own // 16) * 16
    spread = jnp.pad(grad_middle.T.reshape(n_seq, own, length), ((0, 0), (0, own_rows - own), (0, 0)))
    banded = jnp.concatenate(
        [jnp.pad(spread, ((0, 0), (0, 0), (k, taps_count - 1 - k))) for k in range(taps_count)],
        axis=1,
    ).reshape(n_seq * taps_count * own_rows, length + taps_count - 1)
    partial = jnp.dot(banded, padded, preferred_element_type=jnp.float32).astype(jnp.bfloat16)
    partial = partial.reshape(n_seq, taps_count * own_rows, in_ch)
    weight_part = lax.psum_scatter(partial, "seq", scatter_dimension=0, tiled=True)[0]
    n_dp = lax.axis_size("dp")
    copies = lax.all_gather(weight_part, "dp", axis=0, tiled=False).astype(jnp.float32)
    total = copies[0]
    for j in range(1, n_dp):
        total = total + copies[j]
    weight_grad = total.reshape(taps_count, own_rows, in_ch)[:, :own].transpose(1, 0, 2)
    summed = jnp.einsum(
        "lo,oc->cl", grad_ext[4 : 4 + length], kernel[:, 0, :], preferred_element_type=jnp.float32
    )
    for offset in range(1, taps_count):
        summed = summed + jnp.einsum(
            "lo,oc->cl",
            grad_ext[4 - offset : 4 - offset + length],
            kernel[:, offset, :],
            preferred_element_type=jnp.float32,
        )
    groups = summed.astype(jnp.bfloat16).reshape(n_section, -1, length)
    received = lax.all_to_all(groups, "section", 0, 0, tiled=True)
    input_rows = jnp.sum(received.astype(jnp.float32), axis=0).astype(jnp.bfloat16)
    return (weight_grad, input_rows[None])


def solution(mesh):
    return jax.shard_map(
        shards,
        mesh=mesh,
        in_specs=(
            P("dp", "seq", None),
            P("section", None, None),
            P("dp", ("seq", "section"), None),
        ),
        out_specs=(P(("section", "seq"), None, None), P("dp", "section", "seq")),
        check_vma=False,
    )
```

```python
import jax
import jax.numpy as jnp
from jax import lax
from jax.sharding import PartitionSpec as P


def extended(block, sides, width):
    for axis, dim in sides:
        count = lax.axis_size(axis)
        forward = [(i, i + 1) for i in range(count - 1)]
        backward = [(target, source) for source, target in forward]
        low = lax.ppermute(
            lax.slice_in_dim(block, block.shape[dim] - width, None, axis=dim), axis, forward
        )
        high = lax.ppermute(lax.slice_in_dim(block, 0, width, axis=dim), axis, backward)
        block = jnp.concatenate([low, block, high], axis=dim)
    return block


def gelu_slope(values):
    normal_cdf = 0.5 * (1.0 + jax.scipy.special.erf(values * 0.7071067811865476))
    density = jnp.exp(-0.5 * values * values) * 0.3989422804014327
    return normal_cdf + values * density


def shards(signal, kernel, trunk_grad):
    local_signal = signal[0]
    length = local_signal.shape[0]
    taps_count = kernel.shape[1]
    out_ch = kernel.shape[0]
    in_ch = kernel.shape[2]
    n_section = lax.axis_size("section")
    rows = trunk_grad.shape[1]
    grouped = jnp.repeat(trunk_grad[0].reshape(rows, n_section, out_ch), 2, axis=0).transpose(1, 0, 2)
    upsampled = lax.all_to_all(grouped, "section", 0, 0, tiled=True).reshape(2 * rows * n_section, out_ch)
    padded = extended(local_signal, (("seq", 0),), 2)
    stacked = kernel.transpose(1, 0, 2).reshape(taps_count * out_ch, in_ch)
    per_tap = jnp.einsum("jc,tc->jt", stacked, padded, preferred_element_type=jnp.float32)
    linear = per_tap[0:out_ch, 0:length]
    for k in range(1, taps_count):
        linear = linear + per_tap[k * out_ch : (k + 1) * out_ch, k : k + length]
    grad_hidden = 0.5 * upsampled.T.astype(jnp.float32)
    grad_flip = (grad_hidden * gelu_slope(linear)).astype(jnp.bfloat16)
    grad_pre = grad_flip.T
    grad_ext = extended(grad_pre, (("seq", 0),), 2)
    n_seq = lax.axis_size("seq")
    own = out_ch // n_seq
    own_rows = -(-own // 16) * 16
    spread = jnp.pad(grad_flip.reshape(n_seq, own, length), ((0, 0), (0, own_rows - own), (0, 0)))
    banded = jnp.concatenate(
        [jnp.pad(spread, ((0, 0), (0, 0), (k, taps_count - 1 - k))) for k in range(taps_count)],
        axis=1,
    ).reshape(n_seq * taps_count * own_rows, length + taps_count - 1)
    partial = jnp.dot(banded, padded, preferred_element_type=jnp.float32).astype(jnp.bfloat16)
    partial = partial.reshape(n_seq, taps_count * own_rows, in_ch)
    weight_part = lax.psum_scatter(partial, "seq", scatter_dimension=0, tiled=True)[0]
    n_dp = lax.axis_size("dp")
    copies = lax.all_gather(weight_part, "dp", axis=0, tiled=False).astype(jnp.float32)
    total = copies[0]
    for j in range(1, n_dp):
        total = total + copies[j]
    weight_grad = total.reshape(taps_count, own_rows, in_ch)[:, :own].transpose(1, 0, 2)
    summed = jnp.einsum(
        "lo,oc->cl", grad_ext[4 : 4 + length], kernel[:, 0, :], preferred_element_type=jnp.float32
    )
    for offset in range(1, taps_count):
        summed = summed + jnp.einsum(
            "lo,oc->cl",
            grad_ext[4 - offset : 4 - offset + length],
            kernel[:, offset, :],
            preferred_element_type=jnp.float32,
        )
    groups = summed.astype(jnp.bfloat16).reshape(n_section, -1, length)
    received = lax.all_to_all(groups, "section", 0, 0, tiled=True)
    input_rows = jnp.sum(received.astype(jnp.float32), axis=0).astype(jnp.bfloat16)
    return (weight_grad, input_rows[None])


def solution(mesh):
    return jax.shard_map(
        shards,
        mesh=mesh,
        in_specs=(
            P("dp", "seq", None),
            P("section", None, None),
            P("dp", ("seq", "section"), None),
        ),
        out_specs=(P(("section", "seq"), None, None), P("dp", "section", "seq")),
        check_vma=False,
    )
```

```python
import jax
import jax.numpy as jnp
from jax import lax
from jax.sharding import PartitionSpec as P


def extended(block, sides, width):
    for axis, dim in sides:
        count = lax.axis_size(axis)
        forward = [(i, i + 1) for i in range(count - 1)]
        backward = [(target, source) for source, target in forward]
        low = lax.ppermute(
            lax.slice_in_dim(block, block.shape[dim] - width, None, axis=dim), axis, forward
        )
        high = lax.ppermute(lax.slice_in_dim(block, 0, width, axis=dim), axis, backward)
        block = jnp.concatenate([low, block, high], axis=dim)
    return block


def gelu_slope(values):
    normal_cdf = 0.5 * (1.0 + jax.scipy.special.erf(values * 0.7071067811865476))
    density = jnp.exp(-0.5 * values * values) * 0.3989422804014327
    return normal_cdf + values * density


def shards(signal, kernel, trunk_grad):
    local_signal = signal[0]
    length = local_signal.shape[0]
    taps_count = kernel.shape[1]
    out_ch = kernel.shape[0]
    in_ch = kernel.shape[2]
    n_section = lax.axis_size("section")
    rows = trunk_grad.shape[1]
    grouped = jnp.repeat(trunk_grad[0].reshape(rows, n_section, out_ch), 2, axis=0).transpose(1, 0, 2)
    upsampled = lax.all_to_all(grouped, "section", 0, 0, tiled=True).reshape(2 * rows * n_section, out_ch)
    anchor = (grouped[0, 0, 0] * 0).astype(local_signal.dtype)
    padded = extended(local_signal + anchor, (("seq", 0),), 2)
    stacked = kernel.transpose(1, 0, 2).reshape(taps_count * out_ch, in_ch)
    per_tap = jnp.einsum("tc,jc->tj", padded, stacked, preferred_element_type=jnp.float32)
    linear = per_tap[0:length, 0:out_ch]
    for k in range(1, taps_count):
        linear = linear + per_tap[k : k + length, k * out_ch : (k + 1) * out_ch]
    grad_hidden = 0.5 * upsampled.astype(jnp.float32)
    grad_pre = (grad_hidden * gelu_slope(linear)).astype(jnp.bfloat16)
    grad_ext = extended(grad_pre, (("seq", 0),), 2)
    grad_middle = grad_ext[2 : 2 + length]
    n_seq = lax.axis_size("seq")
    own = out_ch // n_seq
    own_rows = -(-own // 16) * 16
    spread = jnp.pad(grad_middle.T.reshape(n_seq, own, length), ((0, 0), (0, own_rows - own), (0, 0)))
    banded = jnp.concatenate(
        [jnp.pad(spread, ((0, 0), (0, 0), (k, taps_count - 1 - k))) for k in range(taps_count)],
        axis=1,
    ).reshape(n_seq * taps_count * own_rows, length + taps_count - 1)
    partial = jnp.dot(banded, padded, preferred_element_type=jnp.float32).astype(jnp.bfloat16)
    partial = partial.reshape(n_seq, taps_count * own_rows, in_ch)
    weight_part = lax.psum_scatter(partial, "seq", scatter_dimension=0, tiled=True)[0]
    n_dp = lax.axis_size("dp")
    copies = lax.all_gather(weight_part, "dp", axis=0, tiled=False).astype(jnp.float32)
    total = copies[0]
    for j in range(1, n_dp):
        total = total + copies[j]
    weight_grad = total.reshape(taps_count, own_rows, in_ch)[:, :own].transpose(1, 0, 2)
    summed = jnp.einsum(
        "lo,oc->cl", grad_ext[4 : 4 + length], kernel[:, 0, :], preferred_element_type=jnp.float32
    )
    for offset in range(1, taps_count):
        summed = summed + jnp.einsum(
            "lo,oc->cl",
            grad_ext[4 - offset : 4 - offset + length],
            kernel[:, offset, :],
            preferred_element_type=jnp.float32,
        )
    groups = summed.astype(jnp.bfloat16).reshape(n_section, -1, length)
    received = lax.all_to_all(groups, "section", 0, 0, tiled=True)
    input_rows = jnp.sum(received.astype(jnp.float32), axis=0).astype(jnp.bfloat16)
    return (weight_grad, input_rows[None])


def solution(mesh):
    return jax.shard_map(
        shards,
        mesh=mesh,
        in_specs=(
            P("dp", "seq", None),
            P("section", None, None),
            P("dp", ("seq", "section"), None),
        ),
        out_specs=(P(("section", "seq"), None, None), P("dp", "section", "seq")),
        check_vma=False,
    )
```

```python
import jax
import jax.numpy as jnp
from jax import lax
from jax.sharding import PartitionSpec as P


def extended(block, sides, width, anchor=None):
    for axis, dim in sides:
        count = lax.axis_size(axis)
        forward = [(i, i + 1) for i in range(count - 1)]
        backward = [(target, source) for source, target in forward]
        tail = lax.slice_in_dim(block, block.shape[dim] - width, None, axis=dim)
        head = lax.slice_in_dim(block, 0, width, axis=dim)
        if anchor is not None:
            tail, head = tail + anchor, head + anchor
        low = lax.ppermute(tail, axis, forward)
        high = lax.ppermute(head, axis, backward)
        block = jnp.concatenate([low, block, high], axis=dim)
    return block


def gelu_slope(values):
    normal_cdf = 0.5 * (1.0 + jax.scipy.special.erf(values * 0.7071067811865476))
    density = jnp.exp(-0.5 * values * values) * 0.3989422804014327
    return normal_cdf + values * density


def shards(signal, kernel, trunk_grad):
    local_signal = signal[0]
    length = local_signal.shape[0]
    taps_count = kernel.shape[1]
    out_ch = kernel.shape[0]
    in_ch = kernel.shape[2]
    n_section = lax.axis_size("section")
    rows = trunk_grad.shape[1]
    grouped = jnp.repeat(trunk_grad[0].reshape(rows, n_section, out_ch), 2, axis=0).transpose(1, 0, 2)
    upsampled = lax.all_to_all(grouped, "section", 0, 0, tiled=True).reshape(2 * rows * n_section, out_ch)
    anchor = (grouped[0, 0, 0] * 0).astype(local_signal.dtype)
    padded = extended(local_signal, (("seq", 0),), 2, anchor)
    stacked = kernel.transpose(1, 0, 2).reshape(taps_count * out_ch, in_ch)
    half = (taps_count - 1) // 2
    per_tap = jnp.pad(
        jnp.einsum("tc,jc->tj", local_signal, stacked, preferred_element_type=jnp.float32),
        ((half, half), (0, 0)),
    )
    edges = jnp.concatenate([padded[:half], padded[length + half :]], axis=0)
    edge_taps = jnp.einsum("tc,jc->tj", edges, stacked, preferred_element_type=jnp.float32)
    top = []
    for r in range(half):
        top.append(sum(edge_taps[r + k, k * out_ch : (k + 1) * out_ch] for k in range(half - r)))
    bottom = []
    for r in range(half):
        t = length - half + r
        terms = [
            edge_taps[half + (t + k - (length + half)), k * out_ch : (k + 1) * out_ch]
            for k in range(taps_count)
            if t + k >= length + half
        ]
        bottom.append(sum(terms))
    correction = jnp.concatenate(
        [jnp.stack(top), jnp.zeros((length - 2 * half, out_ch), jnp.float32), jnp.stack(bottom)], axis=0
    )
    linear = per_tap[0:length, 0:out_ch]
    for k in range(1, taps_count):
        linear = linear + per_tap[k : k + length, k * out_ch : (k + 1) * out_ch]
    linear = linear + correction
    grad_hidden = 0.5 * upsampled.astype(jnp.float32)
    grad_pre = (grad_hidden * gelu_slope(linear)).astype(jnp.bfloat16)
    grad_ext = extended(grad_pre, (("seq", 0),), 2)
    grad_middle = grad_ext[2 : 2 + length]
    n_seq = lax.axis_size("seq")
    own = out_ch // n_seq
    own_rows = -(-own // 16) * 16
    spread = jnp.pad(grad_middle.T.reshape(n_seq, own, length), ((0, 0), (0, own_rows - own), (0, 0)))
    banded = jnp.concatenate(
        [jnp.pad(spread, ((0, 0), (0, 0), (k, taps_count - 1 - k))) for k in range(taps_count)],
        axis=1,
    ).reshape(n_seq * taps_count * own_rows, length + taps_count - 1)
    partial = jnp.dot(banded, padded, preferred_element_type=jnp.float32).astype(jnp.bfloat16)
    partial = partial.reshape(n_seq, taps_count * own_rows, in_ch)
    weight_part = lax.psum_scatter(partial, "seq", scatter_dimension=0, tiled=True)[0]
    n_dp = lax.axis_size("dp")
    copies = lax.all_gather(weight_part, "dp", axis=0, tiled=False).astype(jnp.float32)
    total = copies[0]
    for j in range(1, n_dp):
        total = total + copies[j]
    weight_grad = total.reshape(taps_count, own_rows, in_ch)[:, :own].transpose(1, 0, 2)
    summed = jnp.einsum(
        "lo,oc->cl", grad_ext[4 : 4 + length], kernel[:, 0, :], preferred_element_type=jnp.float32
    )
    for offset in range(1, taps_count):
        summed = summed + jnp.einsum(
            "lo,oc->cl",
            grad_ext[4 - offset : 4 - offset + length],
            kernel[:, offset, :],
            preferred_element_type=jnp.float32,
        )
    groups = summed.astype(jnp.bfloat16).reshape(n_section, -1, length)
    received = lax.all_to_all(groups, "section", 0, 0, tiled=True)
    input_rows = jnp.sum(received.astype(jnp.float32), axis=0).astype(jnp.bfloat16)
    return (weight_grad, input_rows[None])


def solution(mesh):
    return jax.shard_map(
        shards,
        mesh=mesh,
        in_specs=(
            P("dp", "seq", None),
            P("section", None, None),
            P("dp", ("seq", "section"), None),
        ),
        out_specs=(P(("section", "seq"), None, None), P("dp", "section", "seq")),
        check_vma=False,
    )
```

```python
import jax
import jax.numpy as jnp
from jax import lax
from jax.sharding import PartitionSpec as P


def extended(block, sides, width):
    for axis, dim in sides:
        count = lax.axis_size(axis)
        forward = [(i, i + 1) for i in range(count - 1)]
        backward = [(target, source) for source, target in forward]
        low = lax.ppermute(
            lax.slice_in_dim(block, block.shape[dim] - width, None, axis=dim), axis, forward
        )
        high = lax.ppermute(lax.slice_in_dim(block, 0, width, axis=dim), axis, backward)
        block = jnp.concatenate([low, block, high], axis=dim)
    return block


def gelu_slope(values):
    normal_cdf = 0.5 * (1.0 + jax.scipy.special.erf(values * 0.7071067811865476))
    density = jnp.exp(-0.5 * values * values) * 0.3989422804014327
    return normal_cdf + values * density


def shards(signal, kernel, trunk_grad):
    local_signal = signal[0]
    length = local_signal.shape[0]
    taps_count = kernel.shape[1]
    out_ch = kernel.shape[0]
    in_ch = kernel.shape[2]
    n_section = lax.axis_size("section")
    rows = trunk_grad.shape[1]
    grouped = jnp.repeat(trunk_grad[0], 2, axis=0).reshape(2 * rows, n_section, out_ch).transpose(1, 0, 2)
    upsampled = lax.all_to_all(grouped, "section", 0, 0, tiled=True).reshape(2 * rows * n_section, out_ch)
    padded = extended(local_signal, (("seq", 0),), 2)
    stacked = kernel.transpose(1, 0, 2).reshape(taps_count * out_ch, in_ch)
    per_tap = jnp.einsum("tc,jc->tj", padded, stacked, preferred_element_type=jnp.float32)
    linear = per_tap[0:length, 0:out_ch]
    for k in range(1, taps_count):
        linear = linear + per_tap[k : k + length, k * out_ch : (k + 1) * out_ch]
    grad_hidden = 0.5 * upsampled.astype(jnp.float32)
    grad_pre = (grad_hidden * gelu_slope(linear)).astype(jnp.bfloat16)
    grad_ext = extended(grad_pre, (("seq", 0),), 2)
    grad_middle = grad_ext[2 : 2 + length]
    n_seq = lax.axis_size("seq")
    own = out_ch // n_seq
    own_rows = -(-own // 16) * 16
    spread = jnp.pad(grad_middle.T.reshape(n_seq, own, length), ((0, 0), (0, own_rows - own), (0, 0)))
    banded = jnp.concatenate(
        [jnp.pad(spread, ((0, 0), (0, 0), (k, taps_count - 1 - k))) for k in range(taps_count)],
        axis=1,
    ).reshape(n_seq * taps_count * own_rows, length + taps_count - 1)
    partial = jnp.dot(banded, padded, preferred_element_type=jnp.float32).astype(jnp.bfloat16)
    partial = partial.reshape(n_seq, taps_count * own_rows, in_ch)
    weight_part = lax.psum_scatter(partial, "seq", scatter_dimension=0, tiled=True)[0]
    n_dp = lax.axis_size("dp")
    copies = lax.all_gather(weight_part, "dp", axis=0, tiled=False).astype(jnp.float32)
    total = copies[0]
    for j in range(1, n_dp):
        total = total + copies[j]
    weight_grad = total.reshape(taps_count, own_rows, in_ch)[:, :own].transpose(1, 0, 2)
    summed = jnp.einsum(
        "lo,oc->cl", grad_ext[4 : 4 + length], kernel[:, 0, :], preferred_element_type=jnp.float32
    )
    for offset in range(1, taps_count):
        summed = summed + jnp.einsum(
            "lo,oc->cl",
            grad_ext[4 - offset : 4 - offset + length],
            kernel[:, offset, :],
            preferred_element_type=jnp.float32,
        )
    groups = summed.astype(jnp.bfloat16).reshape(n_section, -1, length)
    received = lax.all_to_all(groups, "section", 0, 0, tiled=True)
    input_rows = jnp.sum(received.astype(jnp.float32), axis=0).astype(jnp.bfloat16)
    return (weight_grad, input_rows[None])


def solution(mesh):
    return jax.shard_map(
        shards,
        mesh=mesh,
        in_specs=(
            P("dp", "seq", None),
            P("section", None, None),
            P("dp", ("seq", "section"), None),
        ),
        out_specs=(P(("section", "seq"), None, None), P("dp", "section", "seq")),
        check_vma=False,
    )
```
